256 devices in a mesh: gy: 4 (over y), gx: 64 (over x, z, core).
Axes of the slice: x: 4, y: 4, z: 8, core: 2. Of those that a mesh axis runs over, the one named last changes fastest.
Arguments:
- fields: bfloat16 [4, 16, 131072], P('gy', None, 'gx'), may hold values from -6 to 6
- leaf_inverse: bfloat16 [4, 512, 256, 256], P('gy', 'gx'), may hold values from -0.375 to 0.375
- coupling: bfloat16 [4, 512, 64, 256], P('gy', 'gx'), may hold values from -0.375 to 0.375
- skeleton_index: int32 [4, 512, 64], P('gy', 'gx'), may hold values from 0 to 255, as said below
- up_coef: float32 [4, 192, 4, 512], P('gy', 'gx'), may hold values from -0.5 to 0.5
- down_coef: float32 [4, 192, 4, 512], P('gy', 'gx'), may hold values from -0.5 to 0.5
- merge_own: bfloat16 [4, 192, 512, 512], P('gy', 'gx'), may hold values from -0.1875 to 0.1875
- merge_other: bfloat16 [4, 192, 512, 512], P('gy', 'gx'), may hold values from -0.1875 to 0.1875
- top_inverse: bfloat16 [4, 32768, 512], P('gy', 'gx'), may hold values from -0.1875 to 0.1875
- compress: bfloat16 [4, 2048, 512], P('gy', 'gx'), may hold values from -0.25 to 0.25
- top_couple: bfloat16 [8192, 8192], P(None, ('gy', 'gx')), may hold values from -0.25 to 0.25
Outputs:
- solution: float32 [4, 16, 131072], P('gy', None, 'gx')
The draws below stay inside these ranges and needn't reach their ends.
Inputs may be any that keep to these rules, and one draw needn't show every extreme that they name: `skeleton_index`: the 64 positions of one box are distinct.
All inputs are finite; a program needn't handle non-finite values.
Results may differ from the reference program's by a relative error of at most 0.015.
Values may be sent and summed in bfloat16 or wider, within the bound.
No kernel may reach another device: no remote copies, remote signals or barrier semaphores. Data moves between devices by JAX's collectives and lax.ppermute only.
A program may use at most 64 MiB of HBM per device.

```python
import jax
import jax.numpy as jnp
import numpy as np
from jax import lax

F = 16
Q = 256
K = 64
NBX = 8
KT = 32
LEVELS = 3
M = 512
NPTS = 2048
N_GY = 4
N_GX = 64
DEVICES = 256


def draw_skeleton_index(key, part):
    count = N_GY * N_GX * NBX
    keys = jax.random.split(key, count)
    chosen = jax.vmap(lambda single: jax.random.permutation(single, Q)[:K])(keys)
    return chosen.reshape(N_GY, N_GX * NBX, K).astype(jnp.int32)


def strengthened(values, key, source, target, blocks, factor):
    owner, partner = [(jnp.arange(values.shape[position]) // (values.shape[position] // blocks)).reshape([-1 if axis == position else 1 for axis in range(values.ndim)]) for position in (source, target)]
    chosen = jax.random.permutation(key, blocks)[partner]
    strong = (owner == chosen) | (owner == (partner + blocks // 2) % blocks)
    return jnp.where(strong, factor * values, values)


def block_levels(stream_key, extent, pieces, least, largest):
    def one(dim, blocks):
        heights = jax.random.uniform(jax.random.fold_in(jax.random.fold_in(stream_key, 6), dim), (blocks,), jnp.float32, least / len(pieces), largest / len(pieces))
        return jnp.repeat(jnp.exp(heights), extent[dim] // blocks).reshape((-1,) + (1,) * (len(extent) - dim - 1))

    factor_of = one(*pieces[0])
    for cut in pieces[1:]:
        factor_of = factor_of * one(*cut)
    return factor_of


def centred(stream_key, extent, deviation, bound, pieces=(), held_as=jnp.bfloat16):
    array = jax.random.normal(stream_key, extent, jnp.float32) * deviation
    if len(pieces) > 0:
        array = block_levels(stream_key, extent, pieces, -0.22, 0.18) * array
    return jnp.clip(array, min=-bound, max=bound).astype(held_as)


def heavy_noise(key, shape, width, most, cuts, heavy, held_as=jnp.bfloat16):
    entries = width * jax.random.normal(key, shape, jnp.float32)
    if cuts:
        entries = entries * block_levels(key, shape, cuts, -0.22, 0.18)
    return jnp.clip(strengthened(entries, jax.random.fold_in(key, 3), *heavy), -most, most).astype(held_as)


def setup_inputs(seed: int = 0) -> dict:
    arg_keys = jax.random.split(jax.random.key(seed), 12)
    return {
        "fields": centred(arg_keys[0], (N_GY, F, N_GX * NPTS), 1.0, 6.0, ((0, 4), (2, 64))),
        "leaf_inverse": centred(arg_keys[1], (N_GY, N_GX * NBX, Q, Q), Q ** -0.5, 0.375, ((0, 4), (1, 64))),
        "coupling": centred(arg_keys[2], (N_GY, N_GX * NBX, K, Q), Q ** -0.5, 0.375, ((0, 4), (1, 64))),
        "skeleton_index": draw_skeleton_index(jax.random.fold_in(arg_keys[11], 71), 0),
        "up_coef": jnp.clip(jax.random.uniform(arg_keys[4], (N_GY, N_GX * LEVELS, 4, M), jnp.float32, -0.5, 0.5) * block_levels(arg_keys[4], (N_GY, N_GX * LEVELS, 4, M), ((0, 4), (1, 64)), -0.4, 0.0), -0.5, 0.5),
        "down_coef": jnp.clip(jax.random.uniform(arg_keys[5], (N_GY, N_GX * LEVELS, 4, M), jnp.float32, -0.5, 0.5) * block_levels(arg_keys[5], (N_GY, N_GX * LEVELS, 4, M), ((0, 4), (1, 64)), -0.4, 0.0), -0.5, 0.5),
        "merge_own": centred(arg_keys[6], (N_GY, N_GX * LEVELS, M, M), (2 * M) ** -0.5, 0.1875, ((0, 4), (1, 64))),
        "merge_other": centred(arg_keys[7], (N_GY, N_GX * LEVELS, M, M), (2 * M) ** -0.5, 0.1875, ((0, 4), (1, 64))),
        "top_inverse": centred(arg_keys[8], (N_GY, N_GX * M, M), (2 * M) ** -0.5, 0.1875, ((0, 4), (1, 64))),
        "compress": centred(arg_keys[9], (N_GY, N_GX * KT, M), M ** -0.5, 0.25, ((0, 4), (1, 64))),
        "top_couple": heavy_noise(arg_keys[10], (DEVICES * KT, DEVICES * KT), (DEVICES * KT) ** -0.5, 0.25, ((1, 256),), (0, 1, 256, 6.0)),
    }


def neighbour_mix(state, coefs):
    padded = jnp.pad(state, ((1, 1), (1, 1), (0, 0), (0, 0)))
    above = padded[:-2, 1:-1]
    below = padded[2:, 1:-1]
    left_side = padded[1:-1, :-2]
    right_side = padded[1:-1, 2:]
    total = coefs[:, :, 0][:, :, None, :] * above + coefs[:, :, 1][:, :, None, :] * below
    total = total + coefs[:, :, 2][:, :, None, :] * left_side + coefs[:, :, 3][:, :, None, :] * right_side
    return state - total


def sibling(values, level):
    order = jnp.asarray(np.arange(N_GX) ^ (1 << level), jnp.int32)
    return jnp.take(values, order, axis=1)


def reference(fields, leaf_inverse, coupling, skeleton_index, up_coef, down_coef, merge_own, merge_other, top_inverse, compress, top_couple):
    blocks = fields.reshape(N_GY, F, N_GX, NBX, Q).transpose(0, 2, 1, 3, 4)
    inverse = leaf_inverse.reshape(N_GY, N_GX, NBX, Q, Q).astype(jnp.float32)
    weights = coupling.reshape(N_GY, N_GX, NBX, K, Q).astype(jnp.float32)
    index = skeleton_index.reshape(N_GY, N_GX, NBX, K)
    own = merge_own.reshape(N_GY, N_GX, LEVELS, M, M)
    other = merge_other.reshape(N_GY, N_GX, LEVELS, M, M)
    upc = up_coef.reshape(N_GY, N_GX, LEVELS, 4, M)
    downc = down_coef.reshape(N_GY, N_GX, LEVELS, 4, M)
    topinv = top_inverse.reshape(N_GY, N_GX, M, M).astype(jnp.float32)
    comp = compress.reshape(N_GY, N_GX, KT, M).astype(jnp.float32)

    solved = jnp.einsum('yxfbq,yxbqr->yxfbr', blocks.astype(jnp.float32), inverse).astype(jnp.bfloat16)
    wide_index = jnp.broadcast_to(index[:, :, None], (N_GY, N_GX, F, NBX, K))
    picked = jnp.take_along_axis(blocks, wide_index, axis=4).astype(jnp.float32)
    state = picked - jnp.einsum('yxfbq,yxbkq->yxfbk', lax.optimization_barrier(solved).astype(jnp.float32), weights)
    state = state.reshape(N_GY, N_GX, F, M)

    for level in range(LEVELS):
        mixed = neighbour_mix(state, upc[:, :, level])
        rounded = lax.optimization_barrier(mixed.astype(jnp.bfloat16)).astype(jnp.float32)
        state = jnp.einsum('yxfm,yxmn->yxfn', rounded, own[:, :, level].astype(jnp.float32))
        state = state + jnp.einsum('yxfm,yxmn->yxfn', sibling(rounded, level), other[:, :, level].astype(jnp.float32))

    top_state = lax.optimization_barrier(state.astype(jnp.bfloat16)).astype(jnp.float32)
    small = jnp.einsum('yxfm,yxkm->yxfk', top_state, comp).astype(jnp.bfloat16)
    flat = small.transpose(2, 0, 1, 3).reshape(F, DEVICES * KT)
    coarse = jnp.dot(flat, top_couple, preferred_element_type=jnp.float32)
    coarse = coarse.reshape(F, N_GY, N_GX, KT).transpose(1, 2, 0, 3)
    coarse_round = lax.optimization_barrier(coarse.astype(jnp.bfloat16)).astype(jnp.float32)
    state = jnp.einsum('yxfm,yxmn->yxfn', top_state, topinv) + jnp.einsum('yxfk,yxkm->yxfm', coarse_round, comp)

    for level in reversed(range(LEVELS)):
        rounded = lax.optimization_barrier(state.astype(jnp.bfloat16)).astype(jnp.float32)
        local_part = jnp.einsum('yxfm,yxnm->yxfn', rounded, own[:, :, level].astype(jnp.float32))
        sent = jnp.einsum('yxfm,yxnm->yxfn', rounded, other[:, :, level].astype(jnp.float32))
        mixed = local_part + sibling(sent, level)
        state = neighbour_mix(mixed, downc[:, :, level])

    skel = state.reshape(N_GY, N_GX, F, NBX, K)
    skel_round = lax.optimization_barrier(skel.astype(jnp.bfloat16)).astype(jnp.float32)
    back = jnp.einsum('yxfbk,yxbkq->yxfbq', skel_round, weights).astype(jnp.bfloat16)
    fixed = jnp.einsum('yxfbq,yxbqr->yxfbr', lax.optimization_barrier(back).astype(jnp.float32), inverse)
    onehot = (index[..., None] == jnp.arange(Q, dtype=jnp.int32)).astype(jnp.float32)
    placed = jnp.einsum('yxfbk,yxbkq->yxfbq', skel, onehot, precision=lax.Precision.HIGHEST)
    result = solved.astype(jnp.float32) - fixed + placed
    return result.transpose(0, 2, 1, 3, 4).reshape(N_GY, F, N_GX * NBX * Q)
```

```python
import jax
import jax.numpy as jnp
from jax import lax
from jax.sharding import PartitionSpec as P


def padded_2(shard, sides, width):
    edges = {}
    for axis, dim in sides:
        size, length = (lax.axis_size(axis), shard.shape[dim])
        up = [(i, (i + 1) % size) for i in range(size - 1)]
        last = lax.slice_in_dim(shard, length - width, length, axis=dim)
        leading = lax.slice_in_dim(shard, 0, width, axis=dim)
        edges[dim] = (
            lax.ppermute(last, axis, up),
            lax.ppermute(leading, axis, [(b, a) for a, b in up]),
        )
    done = []
    for _, dim in sides:
        low, high = edges[dim]
        around = [(width, width) if d in done else (0, 0) for d in range(shard.ndim)]
        shard = jnp.concatenate([jnp.pad(low, around), shard, jnp.pad(high, around)], axis=dim)
        done.append(dim)
    return shard


def partner_2(shard, axis, stride):
    return lax.ppermute(shard, axis, [(i, i ^ 1 << stride) for i in range(lax.axis_size(axis))])


def sent_to_all(shard, axis):
    copies = jnp.broadcast_to(shard, (lax.axis_size(axis), *shard.shape))
    return lax.all_to_all(copies, axis, split_axis=0, concat_axis=0, tiled=True)


def joined_along(parts, dim):
    shape = list(parts.shape[1:])
    shape[dim] *= parts.shape[0]
    return jnp.moveaxis(parts, 0, dim).reshape(shape)


def collect(shard, axis, dim):
    parts = sent_to_all(shard, axis)
    return joined_along(parts, dim)


def neighbour_mix(padded, coefs):
    total = coefs[0] * padded[0, 1] + coefs[1] * padded[2, 1]
    return total + coefs[2] * padded[1, 0] + coefs[3] * padded[1, 2]


def right_transpose(values, matrix):
    return lax.dot_general(
        values, matrix, (((1,), (1,)), ((), ())), preferred_element_type=jnp.float32
    )


def body(
    fields,
    leaf_inverse,
    coupling,
    skeleton_index,
    up_coef,
    down_coef,
    merge_own,
    merge_other,
    top_inverse,
    compress,
    top_couple,
):
    field_count = fields.shape[1]
    box_count = leaf_inverse.shape[1]
    box_size = leaf_inverse.shape[2]
    skel_size = coupling.shape[2]
    skel_total = box_count * skel_size
    level_count = merge_own.shape[1]
    blocks = fields[0].reshape(field_count, box_count, box_size)
    inverse = leaf_inverse[0]
    weights = coupling[0]
    index = skeleton_index[0]
    own = merge_own[0]
    other = merge_other[0]
    up_rates = up_coef[0]
    down_rates = down_coef[0]
    positions = lax.broadcasted_iota(jnp.int32, (box_count, skel_size, box_size), 2)
    selector = index[:, :, None] == positions
    select_half = selector.astype(jnp.bfloat16)
    select_full = selector.astype(jnp.float32)
    solved = jnp.einsum("fbq,bqr->fbr", blocks, inverse, preferred_element_type=jnp.float32).astype(
        jnp.bfloat16
    )
    picked = jnp.einsum("fbq,bkq->fbk", blocks, select_half, preferred_element_type=jnp.float32)
    state = picked - jnp.einsum("fbq,bkq->fbk", solved, weights, preferred_element_type=jnp.float32)
    state = state.reshape(field_count, skel_total)
    for level in range(level_count):
        padded = padded_2(state[None, None], (("gy", 0), ("gx", 1)), 1)
        mixed = state - neighbour_mix(padded, up_rates[level])
        rounded = mixed.astype(jnp.bfloat16)
        partner = partner_2(rounded, "gx", level)
        state = jnp.dot(rounded, own[level], preferred_element_type=jnp.float32)
        state = state + jnp.dot(partner, other[level], preferred_element_type=jnp.float32)
    top_state = state.astype(jnp.bfloat16)
    comp = compress[0]
    small = right_transpose(top_state, comp).astype(jnp.bfloat16)
    gathered = lax.all_gather(small, ("gy", "gx"), axis=1, tiled=True)
    coarse = jnp.dot(gathered, top_couple, preferred_element_type=jnp.float32)
    state = jnp.dot(top_state, top_inverse[0], preferred_element_type=jnp.float32)
    state = state + jnp.dot(coarse.astype(jnp.bfloat16), comp, preferred_element_type=jnp.float32)
    for level in reversed(range(level_count)):
        rounded = state.astype(jnp.bfloat16)
        sent = right_transpose(rounded, other[level])
        received = partner_2(sent.astype(jnp.bfloat16), "gx", level).astype(sent.dtype)
        mixed = right_transpose(rounded, own[level]) + received
        padded = padded_2(mixed[None, None].astype(jnp.bfloat16), (("gy", 0), ("gx", 1)), 1).astype(
            jnp.float32
        )
        state = mixed - neighbour_mix(padded, down_rates[level])
    skeleton = state.reshape(field_count, box_count, skel_size)
    back = jnp.einsum(
        "fbk,bkq->fbq", skeleton.astype(jnp.bfloat16), weights, preferred_element_type=jnp.float32
    ).astype(jnp.bfloat16)
    fixed = jnp.einsum("fbq,bqr->fbr", back, inverse, preferred_element_type=jnp.float32)
    placed = jnp.einsum("fbk,bkq->fbq", skeleton, select_full)
    result = solved.astype(jnp.float32) - fixed + placed
    return result.reshape(1, field_count, box_count * box_size)


def solution(mesh):
    placed = (
        P("gy", None, "gx"),
        P("gy", "gx", None, None),
        P("gy", "gx", None, None),
        P("gy", "gx", None),
        P("gy", "gx", None, None),
        P("gy", "gx", None, None),
        P("gy", "gx", None, None),
        P("gy", "gx", None, None),
        P("gy", "gx", None),
        P("gy", "gx", None),
        P(None, ("gy", "gx")),
    )
    return jax.shard_map(
        body, mesh=mesh, in_specs=placed, out_specs=P("gy", None, "gx"), check_vma=False
    )
```

```python
import jax
import jax.numpy as jnp
from jax import lax
from jax.sharding import PartitionSpec as P


def padded_2(shard, sides, width):
    edges = {}
    for axis, dim in sides:
        size, length = (lax.axis_size(axis), shard.shape[dim])
        up = [(i, (i + 1) % size) for i in range(size - 1)]
        last = lax.slice_in_dim(shard, length - width, length, axis=dim)
        leading = lax.slice_in_dim(shard, 0, width, axis=dim)
        edges[dim] = (
            lax.ppermute(last, axis, up),
            lax.ppermute(leading, axis, [(b, a) for a, b in up]),
        )
    done = []
    for _, dim in sides:
        low, high = edges[dim]
        around = [(width, width) if d in done else (0, 0) for d in range(shard.ndim)]
        shard = jnp.concatenate([jnp.pad(low, around), shard, jnp.pad(high, around)], axis=dim)
        done.append(dim)
    return shard


def partner_2(shard, axis, stride):
    return lax.ppermute(shard, axis, [(i, i ^ 1 << stride) for i in range(lax.axis_size(axis))])


def sent_to_all(shard, axis):
    copies = jnp.broadcast_to(shard, (lax.axis_size(axis), *shard.shape))
    return lax.all_to_all(copies, axis, split_axis=0, concat_axis=0, tiled=True)


def joined_along(parts, dim):
    shape = list(parts.shape[1:])
    shape[dim] *= parts.shape[0]
    return jnp.moveaxis(parts, 0, dim).reshape(shape)


def collect(shard, axis, dim):
    parts = sent_to_all(shard, axis)
    return joined_along(parts, dim)


def neighbour_mix(padded, coefs):
    total = coefs[0] * padded[0, 1] + coefs[1] * padded[2, 1]
    return total + coefs[2] * padded[1, 0] + coefs[3] * padded[1, 2]


def right_transpose(values, matrix):
    return lax.dot_general(
        values, matrix, (((1,), (1,)), ((), ())), preferred_element_type=jnp.float32
    )


def body(
    fields,
    leaf_inverse,
    coupling,
    skeleton_index,
    up_coef,
    down_coef,
    merge_own,
    merge_other,
    top_inverse,
    compress,
    top_couple,
):
    field_count = fields.shape[1]
    box_count = leaf_inverse.shape[1]
    box_size = leaf_inverse.shape[2]
    skel_size = coupling.shape[2]
    skel_total = box_count * skel_size
    level_count = merge_own.shape[1]
    blocks = fields[0].reshape(field_count, box_count, box_size)
    inverse = leaf_inverse[0]
    weights = coupling[0]
    index = skeleton_index[0]
    own = merge_own[0]
    other = merge_other[0]
    up_rates = up_coef[0]
    down_rates = down_coef[0]
    positions = lax.broadcasted_iota(jnp.int32, (box_count, skel_size, box_size), 2)
    selector = index[:, :, None] == positions
    select_half = selector.astype(jnp.bfloat16)
    select_full = selector.astype(jnp.float32)
    solved = jnp.einsum("fbq,bqr->fbr", blocks, inverse, preferred_element_type=jnp.float32).astype(
        jnp.bfloat16
    )
    picked = jnp.einsum("fbq,bkq->fbk", blocks, select_half, preferred_element_type=jnp.float32)
    state = picked - jnp.einsum("fbq,bkq->fbk", solved, weights, preferred_element_type=jnp.float32)
    state = state.reshape(field_count, skel_total)
    for level in range(level_count):
        padded = padded_2(state[None, None], (("gy", 0), ("gx", 1)), 1)
        mixed = state - neighbour_mix(padded, up_rates[level])
        rounded = mixed.astype(jnp.bfloat16)
        partner = partner_2(rounded, "gx", level)
        state = jnp.dot(rounded, own[level], preferred_element_type=jnp.float32)
        state = state + jnp.dot(partner, other[level], preferred_element_type=jnp.float32)
    top_state = state.astype(jnp.bfloat16)
    comp = compress[0]
    small = right_transpose(top_state, comp).astype(jnp.bfloat16)
    gathered = collect(small, ("gy", "gx"), 1)
    coarse = jnp.dot(gathered, top_couple, preferred_element_type=jnp.float32)
    state = jnp.dot(top_state, top_inverse[0], preferred_element_type=jnp.float32)
    state = state + jnp.dot(coarse.astype(jnp.bfloat16), comp, preferred_element_type=jnp.float32)
    for level in reversed(range(level_count)):
        rounded = state.astype(jnp.bfloat16)
        sent = right_transpose(rounded, other[level])
        received = partner_2(sent.astype(jnp.bfloat16), "gx", level).astype(sent.dtype)
        mixed = right_transpose(rounded, own[level]) + received
        padded = padded_2(mixed[None, None].astype(jnp.bfloat16), (("gy", 0), ("gx", 1)), 1).astype(
            jnp.float32
        )
        state = mixed - neighbour_mix(padded, down_rates[level])
    skeleton = state.reshape(field_count, box_count, skel_size)
    back = jnp.einsum(
        "fbk,bkq->fbq", skeleton.astype(jnp.bfloat16), weights, preferred_element_type=jnp.float32
    ).astype(jnp.bfloat16)
    fixed = jnp.einsum("fbq,bqr->fbr", back, inverse, preferred_element_type=jnp.float32)
    placed = jnp.einsum("fbk,bkq->fbq", skeleton, select_full)
    result = solved.astype(jnp.float32) - fixed + placed
    return result.reshape(1, field_count, box_count * box_size)


def solution(mesh):
    placed = (
        P("gy", None, "gx"),
        P("gy", "gx", None, None),
        P("gy", "gx", None, None),
        P("gy", "gx", None),
        P("gy", "gx", None, None),
        P("gy", "gx", None, None),
        P("gy", "gx", None, None),
        P("gy", "gx", None, None),
        P("gy", "gx", None),
        P("gy", "gx", None),
        P(None, ("gy", "gx")),
    )
    return jax.shard_map(
        body, mesh=mesh, in_specs=placed, out_specs=P("gy", None, "gx"), check_vma=False
    )
```

```python
import jax
import jax.numpy as jnp
from jax import lax
from jax.sharding import PartitionSpec as P


def padded_2(shard, sides, width):
    edges = {}
    for axis, dim in sides:
        size, length = (lax.axis_size(axis), shard.shape[dim])
        up = [(i, (i + 1) % size) for i in range(size - 1)]
        last = lax.slice_in_dim(shard, length - width, length, axis=dim)
        leading = lax.slice_in_dim(shard, 0, width, axis=dim)
        edges[dim] = (
            lax.ppermute(last, axis, up),
            lax.ppermute(leading, axis, [(b, a) for a, b in up]),
        )
    done = []
    for _, dim in sides:
        low, high = edges[dim]
        around = [(width, width) if d in done else (0, 0) for d in range(shard.ndim)]
        shard = jnp.concatenate([jnp.pad(low, around), shard, jnp.pad(high, around)], axis=dim)
        done.append(dim)
    return shard


def partner_2(shard, axis, stride):
    return lax.ppermute(shard, axis, [(i, i ^ 1 << stride) for i in range(lax.axis_size(axis))])


def sent_to_all(shard, axis):
    copies = jnp.broadcast_to(shard, (lax.axis_size(axis), *shard.shape))
    return lax.all_to_all(copies, axis, split_axis=0, concat_axis=0, tiled=True)


def joined_along(parts, dim):
    shape = list(parts.shape[1:])
    shape[dim] *= parts.shape[0]
    return jnp.moveaxis(parts, 0, dim).reshape(shape)


def collect(shard, axis, dim):
    parts = sent_to_all(shard, axis)
    return joined_along(parts, dim)


def neighbour_mix(padded, coefs):
    total = coefs[0] * padded[0, 1] + coefs[1] * padded[2, 1]
    return total + coefs[2] * padded[1, 0] + coefs[3] * padded[1, 2]


def right_transpose(values, matrix):
    return lax.dot_general(
        values, matrix, (((1,), (1,)), ((), ())), preferred_element_type=jnp.float32
    )


def body(
    fields,
    leaf_inverse,
    coupling,
    skeleton_index,
    up_coef,
    down_coef,
    merge_own,
    merge_other,
    top_inverse,
    compress,
    top_couple,
):
    field_count = fields.shape[1]
    box_count = leaf_inverse.shape[1]
    box_size = leaf_inverse.shape[2]
    skel_size = coupling.shape[2]
    skel_total = box_count * skel_size
    level_count = merge_own.shape[1]
    blocks = fields[0].reshape(field_count, box_count, box_size)
    inverse = leaf_inverse[0]
    weights = coupling[0]
    index = skeleton_index[0]
    own = merge_own[0]
    other = merge_other[0]
    up_rates = up_coef[0]
    down_rates = down_coef[0]
    positions = lax.broadcasted_iota(jnp.int32, (box_count, skel_size, box_size), 2)
    selector = index[:, :, None] == positions
    select_half = selector.astype(jnp.bfloat16)
    select_full = selector.astype(jnp.float32)
    solved = jnp.einsum("fbq,bqr->fbr", blocks, inverse, preferred_element_type=jnp.float32).astype(
        jnp.bfloat16
    )
    picked = jnp.einsum("fbq,bkq->fbk", blocks, select_half, preferred_element_type=jnp.float32)
    state = picked - jnp.einsum("fbq,bkq->fbk", solved, weights, preferred_element_type=jnp.float32)
    state = state.reshape(field_count, skel_total)
    for level in range(level_count):
        padded = padded_2(state[None, None], (("gy", 0), ("gx", 1)), 1)
        mixed = state - neighbour_mix(padded, up_rates[level])
        rounded = mixed.astype(jnp.bfloat16)
        partner = partner_2(rounded, "gx", level)
        state = jnp.dot(rounded, own[level], preferred_element_type=jnp.float32)
        state = state + jnp.dot(partner, other[level], preferred_element_type=jnp.float32)
    top_state = state.astype(jnp.bfloat16)
    comp = compress[0]
    small = right_transpose(top_state, comp).astype(jnp.bfloat16)
    slot = lax.axis_index("gy") * lax.axis_size("gx") + lax.axis_index("gx")
    count = lax.axis_size("gy") * lax.axis_size("gx")
    spread = jnp.zeros((count,) + small.shape, small.dtype)
    spread = lax.dynamic_update_index_in_dim(spread, small, slot, 0)
    summed = lax.psum(spread, ("gy", "gx"))
    gathered = summed.transpose(1, 0, 2).reshape(small.shape[0], -1)
    coarse = jnp.dot(gathered, top_couple, preferred_element_type=jnp.float32)
    state = jnp.dot(top_state, top_inverse[0], preferred_element_type=jnp.float32)
    state = state + jnp.dot(coarse.astype(jnp.bfloat16), comp, preferred_element_type=jnp.float32)
    for level in reversed(range(level_count)):
        rounded = state.astype(jnp.bfloat16)
        sent = right_transpose(rounded, other[level])
        received = partner_2(sent.astype(jnp.bfloat16), "gx", level).astype(sent.dtype)
        mixed = right_transpose(rounded, own[level]) + received
        padded = padded_2(mixed[None, None].astype(jnp.bfloat16), (("gy", 0), ("gx", 1)), 1).astype(
            jnp.float32
        )
        state = mixed - neighbour_mix(padded, down_rates[level])
    skeleton = state.reshape(field_count, box_count, skel_size)
    back = jnp.einsum(
        "fbk,bkq->fbq", skeleton.astype(jnp.bfloat16), weights, preferred_element_type=jnp.float32
    ).astype(jnp.bfloat16)
    fixed = jnp.einsum("fbq,bqr->fbr", back, inverse, preferred_element_type=jnp.float32)
    placed = jnp.einsum("fbk,bkq->fbq", skeleton, select_full)
    result = solved.astype(jnp.float32) - fixed + placed
    return result.reshape(1, field_count, box_count * box_size)


def solution(mesh):
    placed = (
        P("gy", None, "gx"),
        P("gy", "gx", None, None),
        P("gy", "gx", None, None),
        P("gy", "gx", None),
        P("gy", "gx", None, None),
        P("gy", "gx", None, None),
        P("gy", "gx", None, None),
        P("gy", "gx", None, None),
        P("gy", "gx", None),
        P("gy", "gx", None),
        P(None, ("gy", "gx")),
    )
    return jax.shard_map(
        body, mesh=mesh, in_specs=placed, out_specs=P("gy", None, "gx"), check_vma=False
    )
```

```python
import jax
import jax.numpy as jnp
from jax import lax
from jax.sharding import PartitionSpec as P


def padded_2(shard, sides, width):
    edges = {}
    for axis, dim in sides:
        size, length = (lax.axis_size(axis), shard.shape[dim])
        up = [(i, (i + 1) % size) for i in range(size - 1)]
        last = lax.slice_in_dim(shard, length - width, length, axis=dim)
        leading = lax.slice_in_dim(shard, 0, width, axis=dim)
        edges[dim] = (
            lax.ppermute(last, axis, up),
            lax.ppermute(leading, axis, [(b, a) for a, b in up]),
        )
    done = []
    for _, dim in sides:
        low, high = edges[dim]
        around = [(width, width) if d in done else (0, 0) for d in range(shard.ndim)]
        shard = jnp.concatenate([jnp.pad(low, around), shard, jnp.pad(high, around)], axis=dim)
        done.append(dim)
    return shard


def partner_2(shard, axis, stride):
    return lax.ppermute(shard, axis, [(i, i ^ 1 << stride) for i in range(lax.axis_size(axis))])


def sent_to_all(shard, axis):
    copies = jnp.broadcast_to(shard, (lax.axis_size(axis), *shard.shape))
    return lax.all_to_all(copies, axis, split_axis=0, concat_axis=0, tiled=True)


def joined_along(parts, dim):
    shape = list(parts.shape[1:])
    shape[dim] *= parts.shape[0]
    return jnp.moveaxis(parts, 0, dim).reshape(shape)


def collect(shard, axis, dim):
    parts = sent_to_all(shard, axis)
    return joined_along(parts, dim)


def neighbour_mix(padded, coefs):
    total = coefs[0] * padded[0, 1] + coefs[1] * padded[2, 1]
    return total + coefs[2] * padded[1, 0] + coefs[3] * padded[1, 2]


def right_transpose(values, matrix):
    return lax.dot_general(
        values, matrix, (((1,), (1,)), ((), ())), preferred_element_type=jnp.float32
    )


def body(
    fields,
    leaf_inverse,
    coupling,
    skeleton_index,
    up_coef,
    down_coef,
    merge_own,
    merge_other,
    top_inverse,
    compress,
    top_couple,
):
    field_count = fields.shape[1]
    box_count = leaf_inverse.shape[1]
    box_size = leaf_inverse.shape[2]
    skel_size = coupling.shape[2]
    skel_total = box_count * skel_size
    level_count = merge_own.shape[1]
    blocks = fields[0].reshape(field_count, box_count, box_size)
    inverse = leaf_inverse[0]
    weights = coupling[0]
    index = skeleton_index[0]
    own = merge_own[0]
    other = merge_other[0]
    up_rates = up_coef[0]
    down_rates = down_coef[0]
    positions = lax.broadcasted_iota(jnp.int32, (box_count, skel_size, box_size), 2)
    selector = index[:, :, None] == positions
    select_half = selector.astype(jnp.bfloat16)
    select_full = selector.astype(jnp.float32)
    solved = jnp.einsum("fbq,bqr->fbr", blocks, inverse, preferred_element_type=jnp.float32).astype(
        jnp.bfloat16
    )
    picked = jnp.einsum("fbq,bkq->fbk", blocks, select_half, preferred_element_type=jnp.float32)
    state = picked - jnp.einsum("fbq,bkq->fbk", solved, weights, preferred_element_type=jnp.float32)
    state = state.reshape(field_count, skel_total)
    def chain(state):
        for level in range(level_count):
            padded = padded_2(state[None, None], (("gy", 0), ("gx", 1)), 1)
            mixed = state - neighbour_mix(padded, up_rates[level])
            rounded = mixed.astype(jnp.bfloat16)
            partner = partner_2(rounded, "gx", level)
            state = jnp.dot(rounded, own[level], preferred_element_type=jnp.float32)
            state = state + jnp.dot(partner, other[level], preferred_element_type=jnp.float32)
        top_state = state.astype(jnp.bfloat16)
        comp = compress[0]
        small = right_transpose(top_state, comp).astype(jnp.bfloat16)
        row_values = collect(small, "gx", 1)
        coarse = jnp.dot(collect(row_values, "gy", 1), top_couple, preferred_element_type=jnp.float32)
        state = jnp.dot(top_state, top_inverse[0], preferred_element_type=jnp.float32)
        state = state + jnp.dot(coarse.astype(jnp.bfloat16), comp, preferred_element_type=jnp.float32)
        for level in reversed(range(level_count)):
            rounded = state.astype(jnp.bfloat16)
            sent = right_transpose(rounded, other[level])
            received = partner_2(sent.astype(jnp.bfloat16), "gx", level).astype(sent.dtype)
            mixed = right_transpose(rounded, own[level]) + received
            padded = padded_2(mixed[None, None].astype(jnp.bfloat16), (("gy", 0), ("gx", 1)), 1).astype(
                jnp.float32
            )
            state = mixed - neighbour_mix(padded, down_rates[level])
        return state

    half = field_count // 2
    state = jnp.concatenate([chain(state[:half]), chain(state[half:])], axis=0)
    skeleton = state.reshape(field_count, box_count, skel_size)
    back = jnp.einsum(
        "fbk,bkq->fbq", skeleton.astype(jnp.bfloat16), weights, preferred_element_type=jnp.float32
    ).astype(jnp.bfloat16)
    fixed = jnp.einsum("fbq,bqr->fbr", back, inverse, preferred_element_type=jnp.float32)
    placed = jnp.einsum("fbk,bkq->fbq", skeleton, select_full)
    result = solved.astype(jnp.float32) - fixed + placed
    return result.reshape(1, field_count, box_count * box_size)


def solution(mesh):
    placed = (
        P("gy", None, "gx"),
        P("gy", "gx", None, None),
        P("gy", "gx", None, None),
        P("gy", "gx", None),
        P("gy", "gx", None, None),
        P("gy", "gx", None, None),
        P("gy", "gx", None, None),
        P("gy", "gx", None, None),
        P("gy", "gx", None),
        P("gy", "gx", None),
        P(None, ("gy", "gx")),
    )
    return jax.shard_map(
        body, mesh=mesh, in_specs=placed, out_specs=P("gy", None, "gx"), check_vma=False
    )
```

```python
import jax
import jax.numpy as jnp
from jax import lax
from jax.sharding import PartitionSpec as P


def padded_2(shard, sides, width):
    edges = {}
    for axis, dim in sides:
        size, length = (lax.axis_size(axis), shard.shape[dim])
        up = [(i, (i + 1) % size) for i in range(size - 1)]
        last = lax.slice_in_dim(shard, length - width, length, axis=dim)
        leading = lax.slice_in_dim(shard, 0, width, axis=dim)
        edges[dim] = (
            lax.ppermute(last, axis, up),
            lax.ppermute(leading, axis, [(b, a) for a, b in up]),
        )
    done = []
    for _, dim in sides:
        low, high = edges[dim]
        around = [(width, width) if d in done else (0, 0) for d in range(shard.ndim)]
        shard = jnp.concatenate([jnp.pad(low, around), shard, jnp.pad(high, around)], axis=dim)
        done.append(dim)
    return shard


def neighbours_of(shard):
    rows, cols = (lax.axis_size("gy"), lax.axis_size("gx"))
    from_below = lax.ppermute(shard, "gy", [(i, i + 1) for i in range(rows - 1)])
    from_above = lax.ppermute(shard, "gy", [(i + 1, i) for i in range(rows - 1)])
    pairs = [(i, i + 1) if i % 2 else (i, i - 1) for i in range(cols)]
    across = lax.ppermute(shard, "gx", [(a, b) for a, b in pairs if 0 <= b < cols])
    beside = lax.ppermute(shard, "gx", [(i, i ^ 1) for i in range(cols)])
    odd = lax.axis_index("gx") % 2 == 1
    left = jnp.where(odd, beside, across)
    right = jnp.where(odd, across, beside)
    return from_below, from_above, left, right


def neighbour_sum(shard, coefs):
    below, above, left, right = neighbours_of(shard)
    total = coefs[0] * below + coefs[1] * above
    return total + coefs[2] * left + coefs[3] * right


def partner_2(shard, axis, stride):
    return lax.ppermute(shard, axis, [(i, i ^ 1 << stride) for i in range(lax.axis_size(axis))])


def sent_to_all(shard, axis):
    copies = jnp.broadcast_to(shard, (lax.axis_size(axis), *shard.shape))
    return lax.all_to_all(copies, axis, split_axis=0, concat_axis=0, tiled=True)


def joined_along(parts, dim):
    shape = list(parts.shape[1:])
    shape[dim] *= parts.shape[0]
    return jnp.moveaxis(parts, 0, dim).reshape(shape)


def collect(shard, axis, dim):
    parts = sent_to_all(shard, axis)
    return joined_along(parts, dim)


def neighbour_mix(padded, coefs):
    total = coefs[0] * padded[0, 1] + coefs[1] * padded[2, 1]
    return total + coefs[2] * padded[1, 0] + coefs[3] * padded[1, 2]


def right_transpose(values, matrix):
    return lax.dot_general(
        values, matrix, (((1,), (1,)), ((), ())), preferred_element_type=jnp.float32
    )


def body(
    fields,
    leaf_inverse,
    coupling,
    skeleton_index,
    up_coef,
    down_coef,
    merge_own,
    merge_other,
    top_inverse,
    compress,
    top_couple,
):
    field_count = fields.shape[1]
    box_count = leaf_inverse.shape[1]
    box_size = leaf_inverse.shape[2]
    skel_size = coupling.shape[2]
    skel_total = box_count * skel_size
    level_count = merge_own.shape[1]
    blocks = fields[0].reshape(field_count, box_count, box_size)
    inverse = leaf_inverse[0]
    weights = coupling[0]
    index = skeleton_index[0]
    own = merge_own[0]
    other = merge_other[0]
    up_rates = up_coef[0]
    down_rates = down_coef[0]
    positions = lax.broadcasted_iota(jnp.int32, (box_count, skel_size, box_size), 2)
    selector = index[:, :, None] == positions
    select_half = selector.astype(jnp.bfloat16)
    select_full = selector.astype(jnp.float32)
    solved = jnp.einsum("fbq,bqr->fbr", blocks, inverse, preferred_element_type=jnp.float32).astype(
        jnp.bfloat16
    )
    picked = jnp.einsum("fbq,bkq->fbk", blocks, select_half, preferred_element_type=jnp.float32)
    state = picked - jnp.einsum("fbq,bkq->fbk", solved, weights, preferred_element_type=jnp.float32)
    state = state.reshape(field_count, skel_total)
    for level in range(level_count):
        mixed = state - neighbour_sum(state, up_rates[level])
        rounded = mixed.astype(jnp.bfloat16)
        partner = partner_2(rounded, "gx", level)
        state = jnp.dot(rounded, own[level], preferred_element_type=jnp.float32)
        state = state + jnp.dot(partner, other[level], preferred_element_type=jnp.float32)
    top_state = state.astype(jnp.bfloat16)
    comp = compress[0]
    small = right_transpose(top_state, comp).astype(jnp.bfloat16)
    row_values = collect(small, "gx", 1)
    coarse = jnp.dot(collect(row_values, "gy", 1), top_couple, preferred_element_type=jnp.float32)
    state = jnp.dot(top_state, top_inverse[0], preferred_element_type=jnp.float32)
    state = state + jnp.dot(coarse.astype(jnp.bfloat16), comp, preferred_element_type=jnp.float32)
    for level in reversed(range(level_count)):
        rounded = state.astype(jnp.bfloat16)
        sent = right_transpose(rounded, other[level])
        received = partner_2(sent.astype(jnp.bfloat16), "gx", level).astype(sent.dtype)
        mixed = right_transpose(rounded, own[level]) + received
        state = mixed - neighbour_sum(mixed.astype(jnp.bfloat16), down_rates[level])
    skeleton = state.reshape(field_count, box_count, skel_size)
    back = jnp.einsum(
        "fbk,bkq->fbq", skeleton.astype(jnp.bfloat16), weights, preferred_element_type=jnp.float32
    ).astype(jnp.bfloat16)
    fixed = jnp.einsum("fbq,bqr->fbr", back, inverse, preferred_element_type=jnp.float32)
    placed = jnp.einsum("fbk,bkq->fbq", skeleton, select_full)
    result = solved.astype(jnp.float32) - fixed + placed
    return result.reshape(1, field_count, box_count * box_size)


def solution(mesh):
    placed = (
        P("gy", None, "gx"),
        P("gy", "gx", None, None),
        P("gy", "gx", None, None),
        P("gy", "gx", None),
        P("gy", "gx", None, None),
        P("gy", "gx", None, None),
        P("gy", "gx", None, None),
        P("gy", "gx", None, None),
        P("gy", "gx", None),
        P("gy", "gx", None),
        P(None, ("gy", "gx")),
    )
    return jax.shard_map(
        body, mesh=mesh, in_specs=placed, out_specs=P("gy", None, "gx"), check_vma=False
    )
```

```python
import jax
import jax.numpy as jnp
from jax import lax
from jax.sharding import PartitionSpec as P


def padded_2(shard, sides, width):
    edges = {}
    for axis, dim in sides:
        size, length = (lax.axis_size(axis), shard.shape[dim])
        up = [(i, (i + 1) % size) for i in range(size - 1)]
        last = lax.slice_in_dim(shard, length - width, length, axis=dim)
        leading = lax.slice_in_dim(shard, 0, width, axis=dim)
        edges[dim] = (
            lax.ppermute(last, axis, up),
            lax.ppermute(leading, axis, [(b, a) for a, b in up]),
        )
    done = []
    for _, dim in sides:
        low, high = edges[dim]
        around = [(width, width) if d in done else (0, 0) for d in range(shard.ndim)]
        shard = jnp.concatenate([jnp.pad(low, around), shard, jnp.pad(high, around)], axis=dim)
        done.append(dim)
    return shard


def both_sides(shard, axis):
    size = lax.axis_size(axis)
    pairs = [(i, i + 1) if i % 2 else (i, i - 1) for i in range(size)]
    across = lax.ppermute(shard, axis, [(a, b) for a, b in pairs if 0 <= b < size])
    beside = lax.ppermute(shard, axis, [(i, i ^ 1) for i in range(size)])
    odd = lax.axis_index(axis) % 2 == 1
    return jnp.where(odd, beside, across), jnp.where(odd, across, beside)


def neighbours_of(shard):
    from_below, from_above = both_sides(shard, "gy")
    left, right = both_sides(shard, "gx")
    return from_below, from_above, left, right


def neighbour_sum(shard, coefs):
    below, above, left, right = neighbours_of(shard)
    total = coefs[0] * below + coefs[1] * above
    return total + coefs[2] * left + coefs[3] * right


def partner_2(shard, axis, stride):
    return lax.ppermute(shard, axis, [(i, i ^ 1 << stride) for i in range(lax.axis_size(axis))])


def sent_to_all(shard, axis):
    copies = jnp.broadcast_to(shard, (lax.axis_size(axis), *shard.shape))
    return lax.all_to_all(copies, axis, split_axis=0, concat_axis=0, tiled=True)


def joined_along(parts, dim):
    shape = list(parts.shape[1:])
    shape[dim] *= parts.shape[0]
    return jnp.moveaxis(parts, 0, dim).reshape(shape)


def collect(shard, axis, dim):
    parts = sent_to_all(shard, axis)
    return joined_along(parts, dim)


def neighbour_mix(padded, coefs):
    total = coefs[0] * padded[0, 1] + coefs[1] * padded[2, 1]
    return total + coefs[2] * padded[1, 0] + coefs[3] * padded[1, 2]


def right_transpose(values, matrix):
    return lax.dot_general(
        values, matrix, (((1,), (1,)), ((), ())), preferred_element_type=jnp.float32
    )


def body(
    fields,
    leaf_inverse,
    coupling,
    skeleton_index,
    up_coef,
    down_coef,
    merge_own,
    merge_other,
    top_inverse,
    compress,
    top_couple,
):
    field_count = fields.shape[1]
    box_count = leaf_inverse.shape[1]
    box_size = leaf_inverse.shape[2]
    skel_size = coupling.shape[2]
    skel_total = box_count * skel_size
    level_count = merge_own.shape[1]
    blocks = fields[0].reshape(field_count, box_count, box_size)
    inverse = leaf_inverse[0]
    weights = coupling[0]
    index = skeleton_index[0]
    own = merge_own[0]
    other = merge_other[0]
    up_rates = up_coef[0]
    down_rates = down_coef[0]
    positions = lax.broadcasted_iota(jnp.int32, (box_count, skel_size, box_size), 2)
    selector = index[:, :, None] == positions
    select_half = selector.astype(jnp.bfloat16)
    select_full = selector.astype(jnp.float32)
    solved = jnp.einsum("fbq,bqr->fbr", blocks, inverse, preferred_element_type=jnp.float32).astype(
        jnp.bfloat16
    )
    picked = jnp.einsum("fbq,bkq->fbk", blocks, select_half, preferred_element_type=jnp.float32)
    state = picked - jnp.einsum("fbq,bkq->fbk", solved, weights, preferred_element_type=jnp.float32)
    state = state.reshape(field_count, skel_total)
    for level in range(level_count):
        mixed = state - neighbour_sum(state, up_rates[level])
        rounded = mixed.astype(jnp.bfloat16)
        partner = partner_2(rounded, "gx", level)
        state = jnp.dot(rounded, own[level], preferred_element_type=jnp.float32)
        state = state + jnp.dot(partner, other[level], preferred_element_type=jnp.float32)
    top_state = state.astype(jnp.bfloat16)
    comp = compress[0]
    small = right_transpose(top_state, comp).astype(jnp.bfloat16)
    row_values = collect(small, "gx", 1)
    coarse = jnp.dot(collect(row_values, "gy", 1), top_couple, preferred_element_type=jnp.float32)
    state = jnp.dot(top_state, top_inverse[0], preferred_element_type=jnp.float32)
    state = state + jnp.dot(coarse.astype(jnp.bfloat16), comp, preferred_element_type=jnp.float32)
    for level in reversed(range(level_count)):
        rounded = state.astype(jnp.bfloat16)
        sent = right_transpose(rounded, other[level])
        received = partner_2(sent.astype(jnp.bfloat16), "gx", level).astype(sent.dtype)
        mixed = right_transpose(rounded, own[level]) + received
        state = mixed - neighbour_sum(mixed.astype(jnp.bfloat16), down_rates[level])
    skeleton = state.reshape(field_count, box_count, skel_size)
    back = jnp.einsum(
        "fbk,bkq->fbq", skeleton.astype(jnp.bfloat16), weights, preferred_element_type=jnp.float32
    ).astype(jnp.bfloat16)
    fixed = jnp.einsum("fbq,bqr->fbr", back, inverse, preferred_element_type=jnp.float32)
    placed = jnp.einsum("fbk,bkq->fbq", skeleton, select_full)
    result = solved.astype(jnp.float32) - fixed + placed
    return result.reshape(1, field_count, box_count * box_size)


def solution(mesh):
    placed = (
        P("gy", None, "gx"),
        P("gy", "gx", None, None),
        P("gy", "gx", None, None),
        P("gy", "gx", None),
        P("gy", "gx", None, None),
        P("gy", "gx", None, None),
        P("gy", "gx", None, None),
        P("gy", "gx", None, None),
        P("gy", "gx", None),
        P("gy", "gx", None),
        P(None, ("gy", "gx")),
    )
    return jax.shard_map(
        body, mesh=mesh, in_specs=placed, out_specs=P("gy", None, "gx"), check_vma=False
    )
```

```python
import jax
import jax.numpy as jnp
from jax import lax
from jax.sharding import PartitionSpec as P


def padded_2(shard, sides, width):
    edges = {}
    for axis, dim in sides:
        size, length = (lax.axis_size(axis), shard.shape[dim])
        up = [(i, (i + 1) % size) for i in range(size - 1)]
        last = lax.slice_in_dim(shard, length - width, length, axis=dim)
        leading = lax.slice_in_dim(shard, 0, width, axis=dim)
        edges[dim] = (
            lax.ppermute(last, axis, up),
            lax.ppermute(leading, axis, [(b, a) for a, b in up]),
        )
    done = []
    for _, dim in sides:
        low, high = edges[dim]
        around = [(width, width) if d in done else (0, 0) for d in range(shard.ndim)]
        shard = jnp.concatenate([jnp.pad(low, around), shard, jnp.pad(high, around)], axis=dim)
        done.append(dim)
    return shard


def both_sides(shard, axis):
    size = lax.axis_size(axis)
    pairs = [(i, i + 1) if i % 2 else (i, i - 1) for i in range(size)]
    across = lax.ppermute(shard, axis, [(a, b) for a, b in pairs if 0 <= b < size])
    beside = lax.ppermute(shard, axis, [(i, i ^ 1) for i in range(size)])
    odd = lax.axis_index(axis) % 2 == 1
    return jnp.where(odd, beside, across), jnp.where(odd, across, beside)


def neighbours_of(shard):
    from_below, from_above = both_sides(shard, "gy")
    left, right = both_sides(shard, "gx")
    return from_below, from_above, left, right


def neighbour_sum(shard, coefs):
    below, above, left, right = neighbours_of(shard)
    total = coefs[0] * below + coefs[1] * above
    return total + coefs[2] * left + coefs[3] * right


def doubled(shard, axis):
    size = lax.axis_size(axis)
    place = lax.axis_index(axis)
    step = 1
    while step < size:
        other = lax.ppermute(shard, axis, [(i, i ^ step) for i in range(size)])
        upper = (place // step) % 2 == 1
        low = jnp.where(upper, other, shard)
        high = jnp.where(upper, shard, other)
        shard = jnp.concatenate([low, high], axis=1)
        step *= 2
    return shard


def partner_2(shard, axis, stride):
    return lax.ppermute(shard, axis, [(i, i ^ 1 << stride) for i in range(lax.axis_size(axis))])


def sent_to_all(shard, axis):
    copies = jnp.broadcast_to(shard, (lax.axis_size(axis), *shard.shape))
    return lax.all_to_all(copies, axis, split_axis=0, concat_axis=0, tiled=True)


def joined_along(parts, dim):
    shape = list(parts.shape[1:])
    shape[dim] *= parts.shape[0]
    return jnp.moveaxis(parts, 0, dim).reshape(shape)


def collect(shard, axis, dim):
    parts = sent_to_all(shard, axis)
    return joined_along(parts, dim)


def neighbour_mix(padded, coefs):
    total = coefs[0] * padded[0, 1] + coefs[1] * padded[2, 1]
    return total + coefs[2] * padded[1, 0] + coefs[3] * padded[1, 2]


def right_transpose(values, matrix):
    return lax.dot_general(
        values, matrix, (((1,), (1,)), ((), ())), preferred_element_type=jnp.float32
    )


def body(
    fields,
    leaf_inverse,
    coupling,
    skeleton_index,
    up_coef,
    down_coef,
    merge_own,
    merge_other,
    top_inverse,
    compress,
    top_couple,
):
    field_count = fields.shape[1]
    box_count = leaf_inverse.shape[1]
    box_size = leaf_inverse.shape[2]
    skel_size = coupling.shape[2]
    skel_total = box_count * skel_size
    level_count = merge_own.shape[1]
    blocks = fields[0].reshape(field_count, box_count, box_size)
    inverse = leaf_inverse[0]
    weights = coupling[0]
    index = skeleton_index[0]
    own = merge_own[0]
    other = merge_other[0]
    up_rates = up_coef[0]
    down_rates = down_coef[0]
    positions = lax.broadcasted_iota(jnp.int32, (box_count, skel_size, box_size), 2)
    selector = index[:, :, None] == positions
    select_half = selector.astype(jnp.bfloat16)
    select_full = selector.astype(jnp.float32)
    solved = jnp.einsum("fbq,bqr->fbr", blocks, inverse, preferred_element_type=jnp.float32).astype(
        jnp.bfloat16
    )
    picked = jnp.einsum("fbq,bkq->fbk", blocks, select_half, preferred_element_type=jnp.float32)
    state = picked - jnp.einsum("fbq,bkq->fbk", solved, weights, preferred_element_type=jnp.float32)
    state = state.reshape(field_count, skel_total)
    for level in range(level_count):
        mixed = state - neighbour_sum(state, up_rates[level])
        rounded = mixed.astype(jnp.bfloat16)
        partner = partner_2(rounded, "gx", level)
        state = jnp.dot(rounded, own[level], preferred_element_type=jnp.float32)
        state = state + jnp.dot(partner, other[level], preferred_element_type=jnp.float32)
    top_state = state.astype(jnp.bfloat16)
    comp = compress[0]
    small = right_transpose(top_state, comp).astype(jnp.bfloat16)
    gathered = doubled(doubled(small, "gx"), "gy")
    coarse = jnp.dot(gathered, top_couple, preferred_element_type=jnp.float32)
    state = jnp.dot(top_state, top_inverse[0], preferred_element_type=jnp.float32)
    state = state + jnp.dot(coarse.astype(jnp.bfloat16), comp, preferred_element_type=jnp.float32)
    for level in reversed(range(level_count)):
        rounded = state.astype(jnp.bfloat16)
        sent = right_transpose(rounded, other[level])
        received = partner_2(sent.astype(jnp.bfloat16), "gx", level).astype(sent.dtype)
        mixed = right_transpose(rounded, own[level]) + received
        state = mixed - neighbour_sum(mixed.astype(jnp.bfloat16), down_rates[level])
    skeleton = state.reshape(field_count, box_count, skel_size)
    back = jnp.einsum(
        "fbk,bkq->fbq", skeleton.astype(jnp.bfloat16), weights, preferred_element_type=jnp.float32
    ).astype(jnp.bfloat16)
    fixed = jnp.einsum("fbq,bqr->fbr", back, inverse, preferred_element_type=jnp.float32)
    placed = jnp.einsum("fbk,bkq->fbq", skeleton, select_full)
    result = solved.astype(jnp.float32) - fixed + placed
    return result.reshape(1, field_count, box_count * box_size)


def solution(mesh):
    placed = (
        P("gy", None, "gx"),
        P("gy", "gx", None, None),
        P("gy", "gx", None, None),
        P("gy", "gx", None),
        P("gy", "gx", None, None),
        P("gy", "gx", None, None),
        P("gy", "gx", None, None),
        P("gy", "gx", None, None),
        P("gy", "gx", None),
        P("gy", "gx", None),
        P(None, ("gy", "gx")),
    )
    return jax.shard_map(
        body, mesh=mesh, in_specs=placed, out_specs=P("gy", None, "gx"), check_vma=False
    )
```

```python
import jax
import jax.numpy as jnp
from jax import lax
from jax.sharding import PartitionSpec as P


def both_sides(shard, axis, beside=None):
    size = lax.axis_size(axis)
    pairs = [(i, i + 1) if i % 2 else (i, i - 1) for i in range(size)]
    across = lax.ppermute(shard, axis, [(a, b) for a, b in pairs if 0 <= b < size])
    if beside is None:
        beside = lax.ppermute(shard, axis, [(i, i ^ 1) for i in range(size)])
    odd = lax.axis_index(axis) % 2 == 1
    return jnp.where(odd, beside, across), jnp.where(odd, across, beside)


def neighbours_of(shard, beside=None):
    left, right = both_sides(shard, "gx", beside)
    from_below, from_above = both_sides(shard, "gy")
    return from_below, from_above, left, right


def neighbour_sum(shard, coefs, beside=None):
    below, above, left, right = neighbours_of(shard, beside)
    total = coefs[0] * below + coefs[1] * above
    return total + coefs[2] * left + coefs[3] * right


def partner_2(shard, axis, stride):
    return lax.ppermute(shard, axis, [(i, i ^ 1 << stride) for i in range(lax.axis_size(axis))])


def sent_to_all(shard, axis):
    copies = jnp.broadcast_to(shard, (lax.axis_size(axis), *shard.shape))
    return lax.all_to_all(copies, axis, split_axis=0, concat_axis=0, tiled=True)


def joined_along(parts, dim):
    shape = list(parts.shape[1:])
    shape[dim] *= parts.shape[0]
    return jnp.moveaxis(parts, 0, dim).reshape(shape)


def collect(shard, axis, dim):
    parts = sent_to_all(shard, axis)
    return joined_along(parts, dim)


def right_transpose(values, matrix):
    return lax.dot_general(
        values, matrix, (((1,), (1,)), ((), ())), preferred_element_type=jnp.float32
    )


def body(
    fields,
    leaf_inverse,
    coupling,
    skeleton_index,
    up_coef,
    down_coef,
    merge_own,
    merge_other,
    top_inverse,
    compress,
    top_couple,
):
    field_count = fields.shape[1]
    box_count = leaf_inverse.shape[1]
    box_size = leaf_inverse.shape[2]
    skel_size = coupling.shape[2]
    skel_total = box_count * skel_size
    level_count = merge_own.shape[1]
    blocks = fields[0].reshape(field_count, box_count, box_size)
    inverse = leaf_inverse[0]
    weights = coupling[0]
    index = skeleton_index[0]
    own = merge_own[0]
    other = merge_other[0]
    up_rates = up_coef[0]
    down_rates = down_coef[0]
    positions = lax.broadcasted_iota(jnp.int32, (box_count, skel_size, box_size), 2)
    selector = index[:, :, None] == positions
    select_half = selector.astype(jnp.bfloat16)
    select_full = selector.astype(jnp.float32)
    solved = jnp.einsum("fbq,bqr->fbr", blocks, inverse, preferred_element_type=jnp.float32).astype(
        jnp.bfloat16
    )
    picked = jnp.einsum("fbq,bkq->fbk", blocks, select_half, preferred_element_type=jnp.float32)
    state = picked - jnp.einsum("fbq,bkq->fbk", solved, weights, preferred_element_type=jnp.float32)
    state = state.reshape(field_count, skel_total)
    for level in range(level_count):
        mixed = state - neighbour_sum(state, up_rates[level])
        rounded = mixed.astype(jnp.bfloat16)
        partner = partner_2(rounded, "gx", level)
        state = jnp.dot(rounded, own[level], preferred_element_type=jnp.float32)
        state = state + jnp.dot(partner, other[level], preferred_element_type=jnp.float32)
    top_state = state.astype(jnp.bfloat16)
    comp = compress[0]
    small = right_transpose(top_state, comp).astype(jnp.bfloat16)
    row_values = collect(small, "gx", 1)
    coarse = jnp.dot(collect(row_values, "gy", 1), top_couple, preferred_element_type=jnp.float32)
    state = jnp.dot(top_state, top_inverse[0], preferred_element_type=jnp.float32)
    state = state + jnp.dot(coarse.astype(jnp.bfloat16), comp, preferred_element_type=jnp.float32)
    for level in reversed(range(level_count)):
        rounded = state.astype(jnp.bfloat16)
        sent = right_transpose(rounded, other[level]).astype(jnp.bfloat16).astype(jnp.float32)
        local = lax.optimization_barrier(right_transpose(rounded, own[level]))
        if level == 0:
            both = partner_2(jnp.stack([sent, local]), "gx", level)
            mixed = local + both[0]
            beside = (both[1] + sent).astype(jnp.bfloat16)
        else:
            mixed = local + partner_2(sent.astype(jnp.bfloat16), "gx", level).astype(jnp.float32)
            beside = None
        rates = down_rates[level]
        state = mixed - neighbour_sum(mixed.astype(jnp.bfloat16), rates, beside)
    skeleton = state.reshape(field_count, box_count, skel_size)
    back = jnp.einsum(
        "fbk,bkq->fbq", skeleton.astype(jnp.bfloat16), weights, preferred_element_type=jnp.float32
    ).astype(jnp.bfloat16)
    fixed = jnp.einsum("fbq,bqr->fbr", back, inverse, preferred_element_type=jnp.float32)
    placed = jnp.einsum("fbk,bkq->fbq", skeleton, select_full)
    result = solved.astype(jnp.float32) - fixed + placed
    return result.reshape(1, field_count, box_count * box_size)


def solution(mesh):
    placed = (
        P("gy", None, "gx"),
        P("gy", "gx", None, None),
        P("gy", "gx", None, None),
        P("gy", "gx", None),
        P("gy", "gx", None, None),
        P("gy", "gx", None, None),
        P("gy", "gx", None, None),
        P("gy", "gx", None, None),
        P("gy", "gx", None),
        P("gy", "gx", None),
        P(None, ("gy", "gx")),
    )
    return jax.shard_map(
        body, mesh=mesh, in_specs=placed, out_specs=P("gy", None, "gx"), check_vma=False
    )
```

```python
import jax
import jax.numpy as jnp
from jax import lax
from jax.sharding import PartitionSpec as P


def both_sides(shard, axis):
    size = lax.axis_size(axis)
    pairs = [(i, i + 1) if i % 2 else (i, i - 1) for i in range(size)]
    across = lax.ppermute(shard, axis, [(a, b) for a, b in pairs if 0 <= b < size])
    beside = lax.ppermute(shard, axis, [(i, i ^ 1) for i in range(size)])
    odd = lax.axis_index(axis) % 2 == 1
    return jnp.where(odd, beside, across), jnp.where(odd, across, beside)


def neighbours_of(shard):
    left, right = both_sides(shard, "gx")
    from_below, from_above = both_sides(shard, "gy")
    return from_below, from_above, left, right


def neighbour_sum(shard, coefs):
    below, above, left, right = neighbours_of(shard)
    total = coefs[0] * below + coefs[1] * above
    return total + coefs[2] * left + coefs[3] * right


def partner_2(shard, axis, stride):
    return lax.ppermute(shard, axis, [(i, i ^ 1 << stride) for i in range(lax.axis_size(axis))])


def sent_to_all(shard, axis):
    copies = jnp.broadcast_to(shard, (lax.axis_size(axis), *shard.shape))
    return lax.all_to_all(copies, axis, split_axis=0, concat_axis=0, tiled=True)


def joined_along(parts, dim):
    shape = list(parts.shape[1:])
    shape[dim] *= parts.shape[0]
    return jnp.moveaxis(parts, 0, dim).reshape(shape)


def collect(shard, axis, dim):
    parts = sent_to_all(shard, axis)
    return joined_along(parts, dim)


def right_transpose(values, matrix):
    return lax.dot_general(
        values, matrix, (((1,), (1,)), ((), ())), preferred_element_type=jnp.float32
    )


def body(
    fields,
    leaf_inverse,
    coupling,
    skeleton_index,
    up_coef,
    down_coef,
    merge_own,
    merge_other,
    top_inverse,
    compress,
    top_couple,
):
    field_count = fields.shape[1]
    box_count = leaf_inverse.shape[1]
    box_size = leaf_inverse.shape[2]
    skel_size = coupling.shape[2]
    skel_total = box_count * skel_size
    level_count = merge_own.shape[1]
    blocks = fields[0].reshape(field_count, box_count, box_size)
    inverse = leaf_inverse[0]
    weights = coupling[0]
    index = skeleton_index[0]
    own = merge_own[0]
    other = merge_other[0]
    up_rates = up_coef[0]
    down_rates = down_coef[0]
    positions = lax.broadcasted_iota(jnp.int32, (box_count, skel_size, box_size), 2)
    selector = index[:, :, None] == positions
    select_half = selector.astype(jnp.bfloat16)
    select_full = selector.astype(jnp.float32)
    solved = jnp.einsum("fbq,bqr->fbr", blocks, inverse, preferred_element_type=jnp.float32).astype(
        jnp.bfloat16
    )
    picked = jnp.einsum("fbq,bkq->fbk", blocks, select_half, preferred_element_type=jnp.float32)
    state = picked - jnp.einsum("fbq,bkq->fbk", solved, weights, preferred_element_type=jnp.float32)
    state = state.reshape(field_count, skel_total)
    for level in range(level_count):
        mixed = state - neighbour_sum(state.astype(jnp.bfloat16), up_rates[level])
        rounded = mixed.astype(jnp.bfloat16)
        partner = partner_2(rounded, "gx", level)
        state = jnp.dot(rounded, own[level], preferred_element_type=jnp.float32)
        state = state + jnp.dot(partner, other[level], preferred_element_type=jnp.float32)
    top_state = state.astype(jnp.bfloat16)
    comp = compress[0]
    small = right_transpose(top_state, comp).astype(jnp.bfloat16)
    row_values = collect(small, "gx", 1)
    coarse = jnp.dot(collect(row_values, "gy", 1), top_couple, preferred_element_type=jnp.float32)
    state = jnp.dot(top_state, top_inverse[0], preferred_element_type=jnp.float32)
    state = state + jnp.dot(coarse.astype(jnp.bfloat16), comp, preferred_element_type=jnp.float32)
    for level in reversed(range(level_count)):
        rounded = state.astype(jnp.bfloat16)
        sent = right_transpose(rounded, other[level])
        received = partner_2(sent.astype(jnp.bfloat16), "gx", level).astype(sent.dtype)
        mixed = lax.optimization_barrier(right_transpose(rounded, own[level])) + received
        state = mixed - neighbour_sum(mixed.astype(jnp.bfloat16), down_rates[level])
    skeleton = state.reshape(field_count, box_count, skel_size)
    back = jnp.einsum(
        "fbk,bkq->fbq", skeleton.astype(jnp.bfloat16), weights, preferred_element_type=jnp.float32
    ).astype(jnp.bfloat16)
    fixed = jnp.einsum("fbq,bqr->fbr", back, inverse, preferred_element_type=jnp.float32)
    placed = jnp.einsum("fbk,bkq->fbq", skeleton, select_full)
    result = solved.astype(jnp.float32) - fixed + placed
    return result.reshape(1, field_count, box_count * box_size)


def solution(mesh):
    placed = (
        P("gy", None, "gx"),
        P("gy", "gx", None, None),
        P("gy", "gx", None, None),
        P("gy", "gx", None),
        P("gy", "gx", None, None),
        P("gy", "gx", None, None),
        P("gy", "gx", None, None),
        P("gy", "gx", None, None),
        P("gy", "gx", None),
        P("gy", "gx", None),
        P(None, ("gy", "gx")),
    )
    return jax.shard_map(
        body, mesh=mesh, in_specs=placed, out_specs=P("gy", None, "gx"), check_vma=False
    )
```

```python
import jax
import jax.numpy as jnp
from jax import lax
from jax.sharding import Mesh, PartitionSpec as P


GX = ("gxa", "gxb")


def both_sides(shard, axis):
    size = lax.axis_size(axis)
    pairs = [(i, i + 1) if i % 2 else (i, i - 1) for i in range(size)]
    across = lax.ppermute(shard, axis, [(a, b) for a, b in pairs if 0 <= b < size])
    beside = lax.ppermute(shard, axis, [(i, i ^ 1) for i in range(size)])
    odd = lax.axis_index(axis) % 2 == 1
    return jnp.where(odd, beside, across), jnp.where(odd, across, beside)


def neighbours_of(shard):
    left, right = both_sides(shard, GX)
    from_below, from_above = both_sides(shard, "gy")
    return from_below, from_above, left, right


def neighbour_sum(shard, coefs):
    below, above, left, right = neighbours_of(shard)
    total = coefs[0] * below + coefs[1] * above
    return total + coefs[2] * left + coefs[3] * right


def partner_2(shard, axis, stride):
    return lax.ppermute(shard, axis, [(i, i ^ 1 << stride) for i in range(lax.axis_size(axis))])


def sent_to_all(shard, axis):
    copies = jnp.broadcast_to(shard, (lax.axis_size(axis), *shard.shape))
    return lax.all_to_all(copies, axis, split_axis=0, concat_axis=0, tiled=True)


def joined_along(parts, dim):
    shape = list(parts.shape[1:])
    shape[dim] *= parts.shape[0]
    return jnp.moveaxis(parts, 0, dim).reshape(shape)


def collect(shard, axis, dim):
    parts = sent_to_all(shard, axis)
    return joined_along(parts, dim)


def right_transpose(values, matrix):
    return lax.dot_general(
        values, matrix, (((1,), (1,)), ((), ())), preferred_element_type=jnp.float32
    )


def body(
    fields,
    leaf_inverse,
    coupling,
    skeleton_index,
    up_coef,
    down_coef,
    merge_own,
    merge_other,
    top_inverse,
    compress,
    top_couple,
):
    field_count = fields.shape[1]
    box_count = leaf_inverse.shape[1]
    box_size = leaf_inverse.shape[2]
    skel_size = coupling.shape[2]
    skel_total = box_count * skel_size
    level_count = merge_own.shape[1]
    blocks = fields[0].reshape(field_count, box_count, box_size)
    inverse = leaf_inverse[0]
    weights = coupling[0]
    index = skeleton_index[0]
    own = merge_own[0]
    other = merge_other[0]
    up_rates = up_coef[0]
    down_rates = down_coef[0]
    positions = lax.broadcasted_iota(jnp.int32, (box_count, skel_size, box_size), 2)
    selector = index[:, :, None] == positions
    select_half = selector.astype(jnp.bfloat16)
    select_full = selector.astype(jnp.float32)
    solved = jnp.einsum("fbq,bqr->fbr", blocks, inverse, preferred_element_type=jnp.float32).astype(
        jnp.bfloat16
    )
    picked = jnp.einsum("fbq,bkq->fbk", blocks, select_half, preferred_element_type=jnp.float32)
    state = picked - jnp.einsum("fbq,bkq->fbk", solved, weights, preferred_element_type=jnp.float32)
    state = state.reshape(field_count, skel_total)
    for level in range(level_count):
        mixed = state - neighbour_sum(state.astype(jnp.bfloat16), up_rates[level])
        rounded = mixed.astype(jnp.bfloat16)
        partner = partner_2(rounded, GX, level)
        state = jnp.dot(rounded, own[level], preferred_element_type=jnp.float32)
        state = state + jnp.dot(partner, other[level], preferred_element_type=jnp.float32)
    top_state = state.astype(jnp.bfloat16)
    comp = compress[0]
    small = right_transpose(top_state, comp).astype(jnp.bfloat16)
    row_values = collect(small, "gxb", 1)
    gathered = collect(row_values, ("gy", "gxa"), 1)
    coarse = jnp.dot(gathered, top_couple, preferred_element_type=jnp.float32)
    state = jnp.dot(top_state, top_inverse[0], preferred_element_type=jnp.float32)
    state = state + jnp.dot(coarse.astype(jnp.bfloat16), comp, preferred_element_type=jnp.float32)
    for level in reversed(range(level_count)):
        rounded = state.astype(jnp.bfloat16)
        sent = right_transpose(rounded, other[level])
        received = partner_2(sent.astype(jnp.bfloat16), GX, level).astype(sent.dtype)
        mixed = lax.optimization_barrier(right_transpose(rounded, own[level])) + received
        state = mixed - neighbour_sum(mixed.astype(jnp.bfloat16), down_rates[level])
    skeleton = state.reshape(field_count, box_count, skel_size)
    back = jnp.einsum(
        "fbk,bkq->fbq", skeleton.astype(jnp.bfloat16), weights, preferred_element_type=jnp.float32
    ).astype(jnp.bfloat16)
    fixed = jnp.einsum("fbq,bqr->fbr", back, inverse, preferred_element_type=jnp.float32)
    placed = jnp.einsum("fbk,bkq->fbq", skeleton, select_full)
    result = solved.astype(jnp.float32) - fixed + placed
    return result.reshape(1, field_count, box_count * box_size)


def solution(mesh):
    placed = (
        P("gy", None, GX),
        P("gy", GX, None, None),
        P("gy", GX, None, None),
        P("gy", GX, None),
        P("gy", GX, None, None),
        P("gy", GX, None, None),
        P("gy", GX, None, None),
        P("gy", GX, None, None),
        P("gy", GX, None),
        P("gy", GX, None),
        P(None, ("gy",) + GX),
    )
    rows, cols = mesh.devices.shape
    split = Mesh(mesh.devices.reshape(rows, 4, cols // 4), ("gy",) + GX)
    return jax.shard_map(
        body, mesh=split, in_specs=placed, out_specs=P("gy", None, GX), check_vma=False
    )
```
